256 devices in a mesh: shards: 32 (over y, z), tensor: 2 (over core), sections: 4 (over x).
Axes of the slice: x: 4, y: 4, z: 8, core: 2. Of those that a mesh axis runs over, the one named last changes fastest.
Arguments:
- in_inputs: bfloat16 [4, 32, 1, 512, 768], P('sections', 'shards'), may hold values from -6 to 6
- in_cotangents: bfloat16 [4, 32, 1, 512, 1792], P('sections', 'shards', None, None, 'tensor'), may hold values from -1536 to 1536
- out_inputs: bfloat16 [4, 32, 1, 512, 1536], P('sections', 'shards', None, None, 'tensor'), may hold values from -6 to 6
- out_cotangents: bfloat16 [4, 32, 1, 512, 768], P('sections', 'shards'), may hold values from -1536 to 1536
- token_counts: int32 [32, 1], P('shards'), may hold values from 1 to 512, as said below
- in_error: float32 [4, 32, 768, 1792], P('sections', 'shards', None, 'tensor'), may hold values from -3 to 3
- out_error: float32 [4, 32, 1536, 768], P('sections', 'shards', 'tensor'), may hold values from -3 to 3
- in_query: float32 [4, 1792, 32], P('sections', 'tensor'), may hold values from -6 to 6
- out_query: float32 [4, 768, 32], P('sections'), may hold values from -6 to 6
- vec_grads: float32 [4, 32, 10568], P('sections', 'shards', 'tensor'), may hold values from -384 to 384
- in_weight: float32 [4, 768, 1792], P('sections', 'shards', 'tensor'), may hold values from -3 to 3
- in_moment: float32 [4, 768, 1792], P('sections', 'shards', 'tensor'), may hold values from -3 to 3
- out_weight: float32 [4, 1536, 768], P('sections', 'tensor', 'shards'), may hold values from -3 to 3
- out_moment: float32 [4, 1536, 768], P('sections', 'tensor', 'shards'), may hold values from -3 to 3
- vec_weight: float32 [4, 10568], P('sections', 'tensor'), may hold values from -3 to 3
- vec_moment: float32 [4, 10568], P('sections', 'tensor'), may hold values from -3 to 3
Outputs:
- new_in_error: float32 [4, 32, 768, 1792], P('sections', 'shards', None, 'tensor')
- new_out_error: float32 [4, 32, 1536, 768], P('sections', 'shards', 'tensor')
- new_in_weight: float32 [4, 768, 1792], P('sections', 'shards', 'tensor')
- new_in_moment: float32 [4, 768, 1792], P('sections', 'shards', 'tensor')
- new_out_weight: float32 [4, 1536, 768], P('sections', 'tensor', 'shards')
- new_out_moment: float32 [4, 1536, 768], P('sections', 'tensor', 'shards')
- new_vec_weight: float32 [4, 10568], P('sections', 'tensor')
- new_vec_moment: float32 [4, 10568], P('sections', 'tensor')
The draws below stay inside these ranges and needn't reach their ends.
Inputs may be any that keep to these rules, and one draw needn't show every extreme that they name: `token_counts`: each count is between 1 and 512; some micro-batch is full.
All inputs are finite; a program needn't handle non-finite values.
Results may differ from the reference program's by a relative error of at most 0.0003.
Values sent between devices are 32-bit elements; how exact they have to be, the bound alone decides.
No kernel may reach another device: no remote copies, remote signals or barrier semaphores. Data moves between devices by JAX's collectives and lax.ppermute only.
A program may use at most 64 MiB of HBM per device.

```python
import jax
import jax.numpy as jnp
from jax import lax

D = 768
RANK = 32
MB = 1
MB_TOK = 512
INNER = 1536
IN_COLS = 1792
VEC = 10568
REPLICAS = 32
LAYERS = 4


def draw_token_counts(key, part):
    replica = jnp.arange(REPLICAS, dtype=jnp.int32)
    upper = MB_TOK * (5 + 11 * replica // max(REPLICAS - 1, 1)) // 16
    upper = jnp.maximum(upper, 1)
    lower = jnp.maximum(upper // 2, 1)
    spread = jax.random.randint(key, (REPLICAS, MB), 0, 1 << 20)
    counts = lower[:, None] + spread % (upper - lower + 1)[:, None]
    counts = counts.at[REPLICAS - 1, 0].set(MB_TOK)
    return counts.astype(jnp.int32)


def block_scale(rng, dims, cuts, low, top_value):
    factor_of, own = 1.0, jax.random.fold_in(rng, 6)
    for axis_at, blocks in cuts:
        steps = jnp.exp(jax.random.uniform(jax.random.fold_in(own, axis_at), (blocks,), jnp.float32, low / len(cuts), top_value / len(cuts)))
        factor_of = factor_of * jnp.repeat(steps, dims[axis_at] // blocks).reshape([-1 if axis == axis_at else 1 for axis in range(len(dims))])
    return factor_of


def bell_draw(stream_key, shape, width, reach, cuts=(), held_as=jnp.bfloat16):
    array = jax.random.normal(stream_key, shape, jnp.float32) * width
    if len(cuts) > 0:
        array = block_scale(stream_key, shape, cuts, -0.22, 0.18) * array
    return jnp.clip(array, min=-reach, max=reach).astype(held_as)


def setup_inputs(seed: int = 0) -> dict:
    key_of = jax.random.split(jax.random.key(seed), 17)
    return {
        "in_inputs": bell_draw(key_of[0], (LAYERS, REPLICAS, MB, MB_TOK, D), 1.0, 6.0, ((0, 4), (1, 32))),
        "in_cotangents": bell_draw(key_of[1], (LAYERS, REPLICAS, MB, MB_TOK, IN_COLS), 256.0, 1536.0, ((0, 4), (1, 32), (4, 2))),
        "out_inputs": bell_draw(key_of[2], (LAYERS, REPLICAS, MB, MB_TOK, INNER), 1.0, 6.0, ((0, 4), (1, 32), (4, 2))),
        "out_cotangents": bell_draw(key_of[3], (LAYERS, REPLICAS, MB, MB_TOK, D), 256.0, 1536.0, ((0, 4), (1, 32))),
        "token_counts": draw_token_counts(jax.random.fold_in(key_of[16], 71), 0),
        "in_error": bell_draw(key_of[5], (LAYERS, REPLICAS, D, IN_COLS), 0.5, 3.0, ((0, 4), (1, 32), (3, 2)), jnp.float32),
        "out_error": bell_draw(key_of[6], (LAYERS, REPLICAS, INNER, D), 0.5, 3.0, ((0, 4), (1, 32), (2, 2)), jnp.float32),
        "in_query": bell_draw(key_of[7], (LAYERS, IN_COLS, RANK), 1.0, 6.0, ((0, 4), (1, 2)), jnp.float32),
        "out_query": bell_draw(key_of[8], (LAYERS, D, RANK), 1.0, 6.0, ((0, 4),), jnp.float32),
        "vec_grads": bell_draw(key_of[9], (LAYERS, REPLICAS, VEC), 64.0, 384.0, ((0, 4), (1, 32), (2, 2)), jnp.float32),
        "in_weight": bell_draw(key_of[10], (LAYERS, D, IN_COLS), 0.5, 3.0, ((0, 4), (1, 32), (2, 2)), jnp.float32),
        "in_moment": bell_draw(key_of[11], (LAYERS, D, IN_COLS), 0.5, 3.0, ((0, 4), (1, 32), (2, 2)), jnp.float32),
        "out_weight": bell_draw(key_of[12], (LAYERS, INNER, D), 0.5, 3.0, ((0, 4), (1, 2), (2, 32)), jnp.float32),
        "out_moment": bell_draw(key_of[13], (LAYERS, INNER, D), 0.5, 3.0, ((0, 4), (1, 2), (2, 32)), jnp.float32),
        "vec_weight": bell_draw(key_of[14], (LAYERS, VEC), 0.5, 3.0, ((0, 4), (1, 2)), jnp.float32),
        "vec_moment": bell_draw(key_of[15], (LAYERS, VEC), 0.5, 3.0, ((0, 4), (1, 2)), jnp.float32),
    }


def orthonormal(left):
    gram = jnp.dot(left.T, left, precision=lax.Precision.HIGHEST)
    factor = jnp.linalg.cholesky(gram)
    return jax.scipy.linalg.solve_triangular(factor, left.T, lower=True).T

def reference(in_inputs, in_cotangents, out_inputs, out_cotangents, token_counts, in_error, out_error, in_query, out_query, vec_grads, in_weight, in_moment, out_weight, out_moment, vec_weight, vec_moment):
    highest = lax.Precision.HIGHEST
    position = jnp.arange(MB_TOK, dtype=jnp.int32)
    valid = (position[None, None, :] < token_counts[:, :, None]).astype(jnp.bfloat16)
    total = jnp.sum(token_counts).astype(jnp.float32)
    kept = []
    square_sum = jnp.float32(0.0)
    for layer in range(LAYERS):
        feats = in_inputs[layer].reshape(REPLICAS, MB * MB_TOK, D).astype(jnp.float32)
        cots = (in_cotangents[layer] * valid[..., None]).reshape(REPLICAS, MB * MB_TOK, IN_COLS).astype(jnp.float32)
        work_in = jnp.einsum('rnd,rnc->rdc', feats, cots) / total + in_error[layer]
        feats = out_inputs[layer].reshape(REPLICAS, MB * MB_TOK, INNER).astype(jnp.float32)
        cots = (out_cotangents[layer] * valid[..., None]).reshape(REPLICAS, MB * MB_TOK, D).astype(jnp.float32)
        work_out = jnp.einsum('rni,rnd->rid', feats, cots) / total + out_error[layer]
        left_in = jnp.einsum('rdc,ck->dk', work_in, in_query[layer], precision=highest)
        left_out = jnp.einsum('rid,dk->ik', work_out, out_query[layer], precision=highest)
        ortho_in = orthonormal(left_in)
        ortho_out = orthonormal(left_out)
        right_in = jnp.einsum('rdc,dk->ck', work_in, ortho_in, precision=highest) / REPLICAS
        right_out = jnp.einsum('rid,ik->dk', work_out, ortho_out, precision=highest) / REPLICAS
        approx_in = jnp.dot(ortho_in, right_in.T, precision=highest)
        approx_out = jnp.dot(ortho_out, right_out.T, precision=highest)
        vec_mean = lax.optimization_barrier(jnp.sum(vec_grads[layer], axis=0)) / total
        square_sum = square_sum + jnp.sum(right_in * right_in) + jnp.sum(right_out * right_out) + jnp.sum(vec_mean * vec_mean)
        kept.append((work_in - approx_in[None], work_out - approx_out[None], approx_in, approx_out, vec_mean))
    factor = 1024.0 / jnp.sqrt(square_sum + 1e-06)
    new_in_error = jnp.stack([item[0] for item in kept])
    new_out_error = jnp.stack([item[1] for item in kept])
    new_in_moment = 0.9 * in_moment + factor * jnp.stack([item[2] for item in kept])
    new_out_moment = 0.9 * out_moment + factor * jnp.stack([item[3] for item in kept])
    new_vec_moment = 0.9 * vec_moment + factor * jnp.stack([item[4] for item in kept])
    return (new_in_error, new_out_error, in_weight - 0.1 * new_in_moment, new_in_moment, out_weight - 0.1 * new_out_moment, new_out_moment, vec_weight - 0.1 * new_vec_moment, new_vec_moment)
```

```python
import jax
import jax.numpy as jnp
from jax import lax
from jax.sharding import PartitionSpec as P


def triangular_apply(left, gram):
    factor = jnp.linalg.cholesky(gram)
    return jax.scipy.linalg.solve_triangular(factor, left.T, lower=True).T


def gradient(inputs, cotangents, valid):
    width_a = inputs.shape[-1]
    width_b = cotangents.shape[-1]
    masked = cotangents[0, 0] * valid[..., None]
    return lax.dot_general(
        inputs[0, 0].reshape(-1, width_a),
        masked.reshape(-1, width_b),
        (((0,), (0,)), ((), ())),
        preferred_element_type=jnp.float32,
    )


def exchange(tree, axis_name, distance):
    size = lax.axis_size(axis_name)
    perm = [(i, i ^ distance) for i in range(size)]
    return lax.ppermute(tree, axis_name, perm)


def butterfly(tree, axis_name):
    size = lax.axis_size(axis_name)
    distance = 1
    while distance < size:
        other = exchange(tree, axis_name, distance)
        tree = jax.tree.map(lambda a, b: a + b, tree, other)
        distance *= 2
    return tree


def local(
    in_inputs,
    in_cotangents,
    out_inputs,
    out_cotangents,
    token_counts,
    in_error,
    out_error,
    in_query,
    out_query,
    vec_grads,
    in_weight,
    in_moment,
    out_weight,
    out_moment,
    vec_weight,
    vec_moment,
):
    highest = lax.Precision.HIGHEST
    contract = (((0,), (0,)), ((), ()))
    replicas = lax.axis_size("shards")
    shard_index = lax.axis_index("shards")
    position = jnp.arange(in_inputs.shape[3], dtype=jnp.int32)
    valid = (position[None, :] < token_counts[0][:, None]).astype(jnp.bfloat16)
    total = butterfly(jnp.sum(token_counts), "shards").astype(jnp.float32)
    work_in = gradient(in_inputs, in_cotangents, valid) / total + in_error[0, 0]
    work_out = gradient(out_inputs, out_cotangents, valid) / total + out_error[0, 0]
    part_in = jnp.dot(work_in, in_query[0], precision=highest)
    part_out = jnp.dot(work_out, out_query[0], precision=highest)
    vec_part = vec_grads[0, 0]
    part_in, left_out, vec_total = butterfly((part_in, part_out, vec_part), "shards")
    other_in, other_out = exchange((part_in, left_out), "tensor", 1)
    left_in = part_in + other_in
    ortho_in = triangular_apply(left_in, jnp.dot(left_in.T, left_in, precision=highest))
    gram_out = jnp.dot(left_out.T, left_out, precision=highest) + jnp.dot(
        other_out.T, other_out, precision=highest
    )
    ortho_out = triangular_apply(left_out, gram_out)
    right_part_in = lax.dot_general(work_in, ortho_in, contract, precision=highest)
    right_part_out = lax.dot_general(work_out, ortho_out, contract, precision=highest)
    right_in, right_part_out = butterfly((right_part_in, right_part_out), "shards")
    right_in = right_in / replicas
    vec_mean = vec_total / total
    own_square = jnp.sum(right_in * right_in) + jnp.sum(vec_mean * vec_mean)
    other_part_out, other_square = exchange((right_part_out, own_square), "tensor", 1)
    right_out = (right_part_out + other_part_out) / replicas
    layer_square = (own_square + other_square) + jnp.sum(right_out * right_out)
    square_sum = butterfly(layer_square, "sections")
    approx_in = jnp.dot(ortho_in, right_in.T, precision=highest)
    approx_out = jnp.dot(ortho_out, right_out.T, precision=highest)
    new_in_error = (work_in - approx_in)[None, None]
    new_out_error = (work_out - approx_out)[None, None]
    factor = 1024.0 / jnp.sqrt(square_sum + 1e-06)
    row_count = in_weight.shape[1]
    shard_in = lax.dynamic_slice_in_dim(approx_in, shard_index * row_count, row_count, 0)
    col_count = out_weight.shape[2]
    shard_out = lax.dynamic_slice_in_dim(approx_out, shard_index * col_count, col_count, 1)
    new_in_moment = 0.9 * in_moment + factor * shard_in[None]
    new_out_moment = 0.9 * out_moment + factor * shard_out[None]
    new_vec_moment = 0.9 * vec_moment + factor * vec_mean[None]
    return (
        new_in_error,
        new_out_error,
        in_weight - 0.1 * new_in_moment,
        new_in_moment,
        out_weight - 0.1 * new_out_moment,
        new_out_moment,
        vec_weight - 0.1 * new_vec_moment,
        new_vec_moment,
    )


def solution(mesh):
    return jax.shard_map(
        local,
        mesh=mesh,
        in_specs=(
            P("sections", "shards", None, None, None),
            P("sections", "shards", None, None, "tensor"),
            P("sections", "shards", None, None, "tensor"),
            P("sections", "shards", None, None, None),
            P("shards", None),
            P("sections", "shards", None, "tensor"),
            P("sections", "shards", "tensor", None),
            P("sections", "tensor", None),
            P("sections", None, None),
            P("sections", "shards", "tensor"),
            P("sections", "shards", "tensor"),
            P("sections", "shards", "tensor"),
            P("sections", "tensor", "shards"),
            P("sections", "tensor", "shards"),
            P("sections", "tensor"),
            P("sections", "tensor"),
        ),
        out_specs=(
            P("sections", "shards", None, "tensor"),
            P("sections", "shards", "tensor", None),
            P("sections", "shards", "tensor"),
            P("sections", "shards", "tensor"),
            P("sections", "tensor", "shards"),
            P("sections", "tensor", "shards"),
            P("sections", "tensor"),
            P("sections", "tensor"),
        ),
        check_vma=False,
    )
```

```python
import jax
import jax.numpy as jnp
from jax import lax
from jax.sharding import PartitionSpec as P


def triangular_apply(left, gram):
    factor = jnp.linalg.cholesky(gram)
    solved = jax.scipy.linalg.solve_triangular(factor, jnp.swapaxes(left, -1, -2), lower=True)
    return jnp.swapaxes(solved, -1, -2)


def gradient(inputs, cotangents, valid):
    width_a = inputs.shape[-1]
    width_b = cotangents.shape[-1]
    masked = cotangents[0, 0] * valid[..., None]
    return lax.dot_general(
        inputs[0, 0].reshape(-1, width_a),
        masked.reshape(-1, width_b),
        (((0,), (0,)), ((), ())),
        preferred_element_type=jnp.float32,
    )


def exchange(tree, axis_name, distance):
    size = lax.axis_size(axis_name)
    perm = [(i, i ^ distance) for i in range(size)]
    return lax.ppermute(tree, axis_name, perm)


def butterfly(tree, axis_name):
    size = lax.axis_size(axis_name)
    distance = 1
    while distance < size:
        other = exchange(tree, axis_name, distance)
        tree = jax.tree.map(lambda a, b: a + b, tree, other)
        distance *= 2
    return tree


def ordered_total(value, axes):
    size = lax.axis_size(axes)
    index = lax.axis_index(axes)
    got = [value]
    for shift in range(1, size):
        perm = [(i, (i + shift) % size) for i in range(size)]
        got.append(lax.ppermute(value, axes, perm))
    stacked = jnp.stack(got)
    ordered = stacked[(index - jnp.arange(size)) % size]
    result = ordered[0]
    for j in range(1, size):
        result = result + ordered[j]
    return result


def local(
    in_inputs,
    in_cotangents,
    out_inputs,
    out_cotangents,
    token_counts,
    in_error,
    out_error,
    in_query,
    out_query,
    vec_grads,
    in_weight,
    in_moment,
    out_weight,
    out_moment,
    vec_weight,
    vec_moment,
):
    highest = lax.Precision.HIGHEST
    contract = (((0,), (0,)), ((), ()))
    replicas = lax.axis_size("shards")
    shard_index = lax.axis_index("shards")
    position = jnp.arange(in_inputs.shape[3], dtype=jnp.int32)
    valid = (position[None, :] < token_counts[0][:, None]).astype(jnp.bfloat16)
    grad_in = gradient(in_inputs, in_cotangents, valid)
    grad_out = gradient(out_inputs, out_cotangents, valid)
    rank = in_query.shape[-1]
    rows = grad_in.shape[0]
    mats = jnp.concatenate(
        [
            jnp.dot(grad_in, in_query[0], precision=highest),
            jnp.dot(in_error[0, 0], in_query[0], precision=highest),
            jnp.dot(grad_out, out_query[0], precision=highest),
            jnp.dot(out_error[0, 0], out_query[0], precision=highest),
        ],
        axis=1,
    )
    width = mats.shape[1]
    vec_len = vec_grads.shape[-1]
    count = jnp.sum(token_counts).astype(jnp.float32)
    tail = jnp.concatenate([vec_grads[0, 0], count[None]])
    tail_rows = -(-(vec_len + 1) // width)
    tail = jnp.pad(tail, (0, tail_rows * width - vec_len - 1)).reshape(tail_rows, width)
    packed = butterfly(jnp.concatenate([mats, tail], axis=0), "shards")
    tail = packed[rows:].reshape(-1)
    vec_total = tail[:vec_len]
    total = tail[vec_len]
    part_in = packed[:rows, 0:rank] / total + packed[:rows, rank : 2 * rank]
    left_out = packed[:rows, 2 * rank : 3 * rank] / total + packed[:rows, 3 * rank : 4 * rank]
    other = exchange(jnp.concatenate([part_in, left_out], axis=1), "tensor", 1)
    left_in = part_in + other[:, :rank]
    other_out = other[:, rank:]
    gram_in = jnp.dot(left_in.T, left_in, precision=highest)
    gram_out = jnp.dot(left_out.T, left_out, precision=highest) + jnp.dot(
        other_out.T, other_out, precision=highest
    )
    ortho = triangular_apply(jnp.stack([left_in, left_out]), jnp.stack([gram_in, gram_out]))
    ortho_in = ortho[0]
    ortho_out = ortho[1]
    work_in = grad_in / total + in_error[0, 0]
    work_out = grad_out / total + out_error[0, 0]
    right_part_in = lax.dot_general(work_in, ortho_in, contract, precision=highest)
    right_part_out = lax.dot_general(work_out, ortho_out, contract, precision=highest)
    right_part_out = right_part_out + exchange(right_part_out, "tensor", 1)
    cols = right_part_in.shape[0]
    packed = butterfly(jnp.concatenate([right_part_in, right_part_out], axis=0), "shards")
    right_in = packed[:cols] / replicas
    right_out = packed[cols:] / replicas
    vec_mean = vec_total / total
    own_square = jnp.sum(right_in * right_in) + jnp.sum(vec_mean * vec_mean)
    out_square = jnp.sum(right_out * right_out)
    own_square = own_square + jnp.where(lax.axis_index("tensor") == 0, out_square, 0.0)
    square_sum = ordered_total(own_square, ("tensor", "sections"))
    approx_in = jnp.dot(ortho_in, right_in.T, precision=highest)
    approx_out = jnp.dot(ortho_out, right_out.T, precision=highest)
    new_in_error = (work_in - approx_in)[None, None]
    new_out_error = (work_out - approx_out)[None, None]
    factor = 1024.0 / jnp.sqrt(square_sum + 1e-06)
    row_count = in_weight.shape[1]
    shard_in = lax.dynamic_slice_in_dim(approx_in, shard_index * row_count, row_count, 0)
    col_count = out_weight.shape[2]
    shard_out = lax.dynamic_slice_in_dim(approx_out, shard_index * col_count, col_count, 1)
    new_in_moment = 0.9 * in_moment + factor * shard_in[None]
    new_out_moment = 0.9 * out_moment + factor * shard_out[None]
    new_vec_moment = 0.9 * vec_moment + factor * vec_mean[None]
    return (
        new_in_error,
        new_out_error,
        in_weight - 0.1 * new_in_moment,
        new_in_moment,
        out_weight - 0.1 * new_out_moment,
        new_out_moment,
        vec_weight - 0.1 * new_vec_moment,
        new_vec_moment,
    )


def solution(mesh):
    return jax.shard_map(
        local,
        mesh=mesh,
        in_specs=(
            P("sections", "shards", None, None, None),
            P("sections", "shards", None, None, "tensor"),
            P("sections", "shards", None, None, "tensor"),
            P("sections", "shards", None, None, None),
            P("shards", None),
            P("sections", "shards", None, "tensor"),
            P("sections", "shards", "tensor", None),
            P("sections", "tensor", None),
            P("sections", None, None),
            P("sections", "shards", "tensor"),
            P("sections", "shards", "tensor"),
            P("sections", "shards", "tensor"),
            P("sections", "tensor", "shards"),
            P("sections", "tensor", "shards"),
            P("sections", "tensor"),
            P("sections", "tensor"),
        ),
        out_specs=(
            P("sections", "shards", None, "tensor"),
            P("sections", "shards", "tensor", None),
            P("sections", "shards", "tensor"),
            P("sections", "shards", "tensor"),
            P("sections", "tensor", "shards"),
            P("sections", "tensor", "shards"),
            P("sections", "tensor"),
            P("sections", "tensor"),
        ),
        check_vma=False,
    )
```

```python
import jax
import jax.numpy as jnp
from jax import lax
from jax.sharding import PartitionSpec as P


def triangular_apply(left, gram):
    factor = jnp.linalg.cholesky(gram)
    solved = jax.scipy.linalg.solve_triangular(factor, jnp.swapaxes(left, -1, -2), lower=True)
    return jnp.swapaxes(solved, -1, -2)


def gradient(inputs, cotangents, valid):
    width_a = inputs.shape[-1]
    width_b = cotangents.shape[-1]
    masked = cotangents[0, 0] * valid[..., None]
    return lax.dot_general(
        inputs[0, 0].reshape(-1, width_a),
        masked.reshape(-1, width_b),
        (((0,), (0,)), ((), ())),
        preferred_element_type=jnp.float32,
    )


def exchange(tree, axis_name, distance):
    size = lax.axis_size(axis_name)
    perm = [(i, i ^ distance) for i in range(size)]
    return lax.ppermute(tree, axis_name, perm)


def butterfly(tree, axis_name):
    size = lax.axis_size(axis_name)
    distance = 1
    while distance < size:
        other = exchange(tree, axis_name, distance)
        tree = jax.tree.map(lambda a, b: a + b, tree, other)
        distance *= 2
    return tree


def local(
    in_inputs,
    in_cotangents,
    out_inputs,
    out_cotangents,
    token_counts,
    in_error,
    out_error,
    in_query,
    out_query,
    vec_grads,
    in_weight,
    in_moment,
    out_weight,
    out_moment,
    vec_weight,
    vec_moment,
):
    highest = lax.Precision.HIGHEST
    contract = (((0,), (0,)), ((), ()))
    replicas = lax.axis_size("shards")
    shard_index = lax.axis_index("shards")
    position = jnp.arange(in_inputs.shape[3], dtype=jnp.int32)
    valid = (position[None, :] < token_counts[0][:, None]).astype(jnp.bfloat16)
    grad_in = gradient(in_inputs, in_cotangents, valid)
    grad_out = gradient(out_inputs, out_cotangents, valid)
    grad_q_in = jnp.dot(grad_in, in_query[0], precision=highest)
    error_q_in = jnp.dot(in_error[0, 0], in_query[0], precision=highest)
    grad_q_out = jnp.dot(grad_out, out_query[0], precision=highest)
    error_q_out = jnp.dot(out_error[0, 0], out_query[0], precision=highest)
    vec_len = vec_grads.shape[-1]
    count = jnp.sum(token_counts).astype(jnp.float32)
    summed = butterfly(jnp.concatenate([vec_grads[0, 0], count[None]]), "shards")
    vec_total = summed[:vec_len]
    total = summed[vec_len]
    part_in = grad_q_in / total + error_q_in
    part_out = grad_q_out / total + error_q_out
    part_in, left_out = butterfly((part_in, part_out), "shards")
    rank = part_in.shape[1]
    other = exchange(jnp.concatenate([part_in, left_out], axis=1), "tensor", 1)
    left_in = part_in + other[:, :rank]
    other_out = other[:, rank:]
    gram_in = jnp.dot(left_in.T, left_in, precision=highest)
    gram_out = jnp.dot(left_out.T, left_out, precision=highest) + jnp.dot(
        other_out.T, other_out, precision=highest
    )
    ortho = triangular_apply(jnp.stack([left_in, left_out]), jnp.stack([gram_in, gram_out]))
    ortho_in = ortho[0]
    ortho_out = ortho[1]
    work_in = grad_in / total + in_error[0, 0]
    work_out = grad_out / total + out_error[0, 0]
    right_part_in = lax.dot_general(work_in, ortho_in, contract, precision=highest)
    right_part_out = lax.dot_general(work_out, ortho_out, contract, precision=highest)
    right_part_out = right_part_out + exchange(right_part_out, "tensor", 1)
    right_in, right_out = butterfly((right_part_in, right_part_out), "shards")
    right_in = right_in / replicas
    right_out = right_out / replicas
    vec_mean = vec_total / total
    own_square = jnp.sum(right_in * right_in) + jnp.sum(vec_mean * vec_mean)
    out_square = jnp.sum(right_out * right_out)
    own_square = own_square + jnp.where(lax.axis_index("tensor") == 0, out_square, 0.0)
    square_sum = butterfly(butterfly(own_square, "tensor"), "sections")
    approx_in = jnp.dot(ortho_in, right_in.T, precision=highest)
    approx_out = jnp.dot(ortho_out, right_out.T, precision=highest)
    new_in_error = (work_in - approx_in)[None, None]
    new_out_error = (work_out - approx_out)[None, None]
    factor = 1024.0 / jnp.sqrt(square_sum + 1e-06)
    row_count = in_weight.shape[1]
    shard_in = lax.dynamic_slice_in_dim(approx_in, shard_index * row_count, row_count, 0)
    col_count = out_weight.shape[2]
    shard_out = lax.dynamic_slice_in_dim(approx_out, shard_index * col_count, col_count, 1)
    new_in_moment = 0.9 * in_moment + factor * shard_in[None]
    new_out_moment = 0.9 * out_moment + factor * shard_out[None]
    new_vec_moment = 0.9 * vec_moment + factor * vec_mean[None]
    return (
        new_in_error,
        new_out_error,
        in_weight - 0.1 * new_in_moment,
        new_in_moment,
        out_weight - 0.1 * new_out_moment,
        new_out_moment,
        vec_weight - 0.1 * new_vec_moment,
        new_vec_moment,
    )


def solution(mesh):
    return jax.shard_map(
        local,
        mesh=mesh,
        in_specs=(
            P("sections", "shards", None, None, None),
            P("sections", "shards", None, None, "tensor"),
            P("sections", "shards", None, None, "tensor"),
            P("sections", "shards", None, None, None),
            P("shards", None),
            P("sections", "shards", None, "tensor"),
            P("sections", "shards", "tensor", None),
            P("sections", "tensor", None),
            P("sections", None, None),
            P("sections", "shards", "tensor"),
            P("sections", "shards", "tensor"),
            P("sections", "shards", "tensor"),
            P("sections", "tensor", "shards"),
            P("sections", "tensor", "shards"),
            P("sections", "tensor"),
            P("sections", "tensor"),
        ),
        out_specs=(
            P("sections", "shards", None, "tensor"),
            P("sections", "shards", "tensor", None),
            P("sections", "shards", "tensor"),
            P("sections", "shards", "tensor"),
            P("sections", "tensor", "shards"),
            P("sections", "tensor", "shards"),
            P("sections", "tensor"),
            P("sections", "tensor"),
        ),
        check_vma=False,
    )
```

```python
import jax
import jax.numpy as jnp
from jax import lax
from jax.sharding import PartitionSpec as P


def triangular_apply(left, gram):
    factor = jnp.linalg.cholesky(gram)
    solved = jax.scipy.linalg.solve_triangular(factor, jnp.swapaxes(left, -1, -2), lower=True)
    return jnp.swapaxes(solved, -1, -2)


def gradient(inputs, cotangents, valid):
    width_a = inputs.shape[-1]
    width_b = cotangents.shape[-1]
    masked = cotangents[0, 0] * valid[..., None]
    return lax.dot_general(
        masked.reshape(-1, width_b),
        inputs[0, 0].reshape(-1, width_a),
        (((0,), (0,)), ((), ())),
        preferred_element_type=jnp.float32,
    ).T


def exchange(tree, axis_name, distance):
    size = lax.axis_size(axis_name)
    perm = [(i, i ^ distance) for i in range(size)]
    return lax.ppermute(tree, axis_name, perm)


def butterfly(tree, axis_name):
    size = lax.axis_size(axis_name)
    distance = 1
    while distance < size:
        other = exchange(tree, axis_name, distance)
        tree = jax.tree.map(lambda a, b: a + b, tree, other)
        distance *= 2
    return tree


def local(
    in_inputs,
    in_cotangents,
    out_inputs,
    out_cotangents,
    token_counts,
    in_error,
    out_error,
    in_query,
    out_query,
    vec_grads,
    in_weight,
    in_moment,
    out_weight,
    out_moment,
    vec_weight,
    vec_moment,
):
    highest = lax.Precision.HIGHEST
    replicas = lax.axis_size("shards")
    shard_index = lax.axis_index("shards")
    position = jnp.arange(in_inputs.shape[3], dtype=jnp.int32)
    valid = (position[None, :] < token_counts[0][:, None]).astype(jnp.bfloat16)
    grad_in = gradient(in_inputs, in_cotangents, valid)
    grad_out = gradient(out_inputs, out_cotangents, valid)
    grad_q_in = jnp.dot(grad_in, in_query[0], precision=highest)
    error_q_in = jnp.dot(in_error[0, 0], in_query[0], precision=highest)
    grad_q_out = jnp.dot(grad_out, out_query[0], precision=highest)
    error_q_out = jnp.dot(out_error[0, 0], out_query[0], precision=highest)
    vec_len = vec_grads.shape[-1]
    count = jnp.sum(token_counts).astype(jnp.float32)
    summed = butterfly(jnp.concatenate([vec_grads[0, 0], count[None]]), "shards")
    vec_total = summed[:vec_len]
    total = summed[vec_len]
    part_in = grad_q_in / total + error_q_in
    part_out = grad_q_out / total + error_q_out
    part_in, left_out = butterfly((part_in, part_out), "shards")
    rank = part_in.shape[1]
    other = exchange(jnp.concatenate([part_in, left_out], axis=1), "tensor", 1)
    left_in = part_in + other[:, :rank]
    other_out = other[:, rank:]
    gram_in = jnp.dot(left_in.T, left_in, precision=highest)
    gram_out = jnp.dot(left_out.T, left_out, precision=highest) + jnp.dot(
        other_out.T, other_out, precision=highest
    )
    ortho = triangular_apply(jnp.stack([left_in, left_out]), jnp.stack([gram_in, gram_out]))
    ortho_in = ortho[0]
    ortho_out = ortho[1]
    work_in = grad_in / total + in_error[0, 0]
    work_out = grad_out / total + out_error[0, 0]
    right_part_in = jnp.dot(ortho_in.T, work_in, precision=highest)
    right_part_out = jnp.dot(ortho_out.T, work_out, precision=highest)
    right_part_out = right_part_out + exchange(right_part_out, "tensor", 1)
    right_in, right_out = butterfly((right_part_in, right_part_out), "shards")
    right_in = right_in / replicas
    right_out = right_out / replicas
    vec_mean = vec_total / total
    own_square = jnp.sum(right_in * right_in) + jnp.sum(vec_mean * vec_mean)
    out_square = jnp.sum(right_out * right_out)
    own_square = own_square + jnp.where(lax.axis_index("tensor") == 0, out_square, 0.0)
    own_square, right_in, right_out = lax.optimization_barrier((own_square, right_in, right_out))
    square_sum = butterfly(butterfly(own_square, "tensor"), "sections")
    approx_in = jnp.dot(ortho_in, right_in, precision=highest)
    approx_out = jnp.dot(ortho_out, right_out, precision=highest)
    new_in_error = (work_in - approx_in)[None, None]
    new_out_error = (work_out - approx_out)[None, None]
    factor = 1024.0 / jnp.sqrt(square_sum + 1e-06)
    row_count = in_weight.shape[1]
    shard_in = lax.dynamic_slice_in_dim(approx_in, shard_index * row_count, row_count, 0)
    col_count = out_weight.shape[2]
    shard_out = lax.dynamic_slice_in_dim(approx_out, shard_index * col_count, col_count, 1)
    new_in_moment = 0.9 * in_moment + factor * shard_in[None]
    new_out_moment = 0.9 * out_moment + factor * shard_out[None]
    new_vec_moment = 0.9 * vec_moment + factor * vec_mean[None]
    return (
        new_in_error,
        new_out_error,
        in_weight - 0.1 * new_in_moment,
        new_in_moment,
        out_weight - 0.1 * new_out_moment,
        new_out_moment,
        vec_weight - 0.1 * new_vec_moment,
        new_vec_moment,
    )


def solution(mesh):
    return jax.shard_map(
        local,
        mesh=mesh,
        in_specs=(
            P("sections", "shards", None, None, None),
            P("sections", "shards", None, None, "tensor"),
            P("sections", "shards", None, None, "tensor"),
            P("sections", "shards", None, None, None),
            P("shards", None),
            P("sections", "shards", None, "tensor"),
            P("sections", "shards", "tensor", None),
            P("sections", "tensor", None),
            P("sections", None, None),
            P("sections", "shards", "tensor"),
            P("sections", "shards", "tensor"),
            P("sections", "shards", "tensor"),
            P("sections", "tensor", "shards"),
            P("sections", "tensor", "shards"),
            P("sections", "tensor"),
            P("sections", "tensor"),
        ),
        out_specs=(
            P("sections", "shards", None, "tensor"),
            P("sections", "shards", "tensor", None),
            P("sections", "shards", "tensor"),
            P("sections", "shards", "tensor"),
            P("sections", "tensor", "shards"),
            P("sections", "tensor", "shards"),
            P("sections", "tensor"),
            P("sections", "tensor"),
        ),
        check_vma=False,
    )
```

```python
import jax
import jax.numpy as jnp
from jax import lax
from jax.sharding import PartitionSpec as P


def triangular_apply(left, gram):
    factor = jnp.linalg.cholesky(gram)
    solved = jax.scipy.linalg.solve_triangular(factor, jnp.swapaxes(left, -1, -2), lower=True)
    return jnp.swapaxes(solved, -1, -2)


def gradient(inputs, cotangents, valid):
    width_a = inputs.shape[-1]
    width_b = cotangents.shape[-1]
    masked = cotangents[0, 0] * valid[..., None]
    return lax.dot_general(
        masked.reshape(-1, width_b),
        inputs[0, 0].reshape(-1, width_a),
        (((0,), (0,)), ((), ())),
        preferred_element_type=jnp.float32,
    ).T


def exchange(tree, axis_name, distance):
    size = lax.axis_size(axis_name)
    perm = [(i, i ^ distance) for i in range(size)]
    return lax.ppermute(tree, axis_name, perm)


def butterfly(tree, axis_name):
    size = lax.axis_size(axis_name)
    distance = 1
    while distance < size:
        other = exchange(tree, axis_name, distance)
        tree = jax.tree.map(lambda a, b: a + b, tree, other)
        distance *= 2
    return tree


def ordered_total(value, axes):
    size = lax.axis_size(axes)
    index = lax.axis_index(axes)
    got = [value]
    for shift in range(1, size):
        perm = [(i, (i + shift) % size) for i in range(size)]
        got.append(lax.ppermute(value, axes, perm))
    stacked = jnp.stack(got)
    ordered = stacked[(index - jnp.arange(size)) % size]
    result = ordered[0]
    for j in range(1, size):
        result = result + ordered[j]
    return result


def local(
    in_inputs,
    in_cotangents,
    out_inputs,
    out_cotangents,
    token_counts,
    in_error,
    out_error,
    in_query,
    out_query,
    vec_grads,
    in_weight,
    in_moment,
    out_weight,
    out_moment,
    vec_weight,
    vec_moment,
):
    highest = lax.Precision.HIGHEST
    replicas = lax.axis_size("shards")
    shard_index = lax.axis_index("shards")
    position = jnp.arange(in_inputs.shape[3], dtype=jnp.int32)
    valid = (position[None, :] < token_counts[0][:, None]).astype(jnp.bfloat16)
    grad_in = gradient(in_inputs, in_cotangents, valid)
    grad_out = gradient(out_inputs, out_cotangents, valid)
    grad_q_in = jnp.dot(grad_in, in_query[0], precision=highest)
    error_q_in = jnp.dot(in_error[0, 0], in_query[0], precision=highest)
    grad_q_out = jnp.dot(grad_out, out_query[0], precision=highest)
    error_q_out = jnp.dot(out_error[0, 0], out_query[0], precision=highest)
    vec_len = vec_grads.shape[-1]
    count = jnp.sum(token_counts).astype(jnp.float32)
    summed = butterfly(jnp.concatenate([vec_grads[0, 0], count[None]]), "shards")
    vec_total = summed[:vec_len]
    total = summed[vec_len]
    part_in = grad_q_in / total + error_q_in
    part_out = grad_q_out / total + error_q_out
    part_in, left_out = butterfly((part_in, part_out), "shards")
    rank = part_in.shape[1]
    other = exchange(jnp.concatenate([part_in, left_out], axis=1), "tensor", 1)
    left_in = part_in + other[:, :rank]
    other_out = other[:, rank:]
    gram_in = jnp.dot(left_in.T, left_in, precision=highest)
    gram_out = jnp.dot(left_out.T, left_out, precision=highest) + jnp.dot(
        other_out.T, other_out, precision=highest
    )
    ortho = triangular_apply(jnp.stack([left_in, left_out]), jnp.stack([gram_in, gram_out]))
    ortho_in = ortho[0]
    ortho_out = ortho[1]
    work_in = grad_in / total + in_error[0, 0]
    work_out = grad_out / total + out_error[0, 0]
    right_part_in = jnp.dot(ortho_in.T, work_in, precision=highest)
    right_part_out = jnp.dot(ortho_out.T, work_out, precision=highest)
    right_part_out = right_part_out + exchange(right_part_out, "tensor", 1)
    right_in, right_out = butterfly((right_part_in, right_part_out), "shards")
    right_in = right_in / replicas
    right_out = right_out / replicas
    vec_mean = vec_total / total
    own_square = jnp.sum(right_in * right_in) + jnp.sum(vec_mean * vec_mean)
    out_square = jnp.sum(right_out * right_out)
    own_square = own_square + jnp.where(lax.axis_index("tensor") == 0, out_square, 0.0)
    own_square, right_in, right_out = lax.optimization_barrier((own_square, right_in, right_out))
    square_sum = ordered_total(own_square, ("tensor", "sections"))
    approx_in = jnp.dot(ortho_in, right_in, precision=highest)
    approx_out = jnp.dot(ortho_out, right_out, precision=highest)
    new_in_error = (work_in - approx_in)[None, None]
    new_out_error = (work_out - approx_out)[None, None]
    factor = 1024.0 / jnp.sqrt(square_sum + 1e-06)
    row_count = in_weight.shape[1]
    shard_in = lax.dynamic_slice_in_dim(approx_in, shard_index * row_count, row_count, 0)
    col_count = out_weight.shape[2]
    shard_out = lax.dynamic_slice_in_dim(approx_out, shard_index * col_count, col_count, 1)
    new_in_moment = 0.9 * in_moment + factor * shard_in[None]
    new_out_moment = 0.9 * out_moment + factor * shard_out[None]
    new_vec_moment = 0.9 * vec_moment + factor * vec_mean[None]
    return (
        new_in_error,
        new_out_error,
        in_weight - 0.1 * new_in_moment,
        new_in_moment,
        out_weight - 0.1 * new_out_moment,
        new_out_moment,
        vec_weight - 0.1 * new_vec_moment,
        new_vec_moment,
    )


def solution(mesh):
    return jax.shard_map(
        local,
        mesh=mesh,
        in_specs=(
            P("sections", "shards", None, None, None),
            P("sections", "shards", None, None, "tensor"),
            P("sections", "shards", None, None, "tensor"),
            P("sections", "shards", None, None, None),
            P("shards", None),
            P("sections", "shards", None, "tensor"),
            P("sections", "shards", "tensor", None),
            P("sections", "tensor", None),
            P("sections", None, None),
            P("sections", "shards", "tensor"),
            P("sections", "shards", "tensor"),
            P("sections", "shards", "tensor"),
            P("sections", "tensor", "shards"),
            P("sections", "tensor", "shards"),
            P("sections", "tensor"),
            P("sections", "tensor"),
        ),
        out_specs=(
            P("sections", "shards", None, "tensor"),
            P("sections", "shards", "tensor", None),
            P("sections", "shards", "tensor"),
            P("sections", "shards", "tensor"),
            P("sections", "tensor", "shards"),
            P("sections", "tensor", "shards"),
            P("sections", "tensor"),
            P("sections", "tensor"),
        ),
        check_vma=False,
    )
```

```python
import jax
import jax.numpy as jnp
from jax import lax
from jax.sharding import PartitionSpec as P


def triangular_apply(left, gram):
    factor = jnp.linalg.cholesky(gram)
    solved = jax.scipy.linalg.solve_triangular(factor, jnp.swapaxes(left, -1, -2), lower=True)
    return jnp.swapaxes(solved, -1, -2)


def gradient(inputs, cotangents, valid):
    width_a = inputs.shape[-1]
    width_b = cotangents.shape[-1]
    masked = cotangents[0, 0] * valid[..., None]
    return lax.dot_general(
        masked.reshape(-1, width_b),
        inputs[0, 0].reshape(-1, width_a),
        (((0,), (0,)), ((), ())),
        preferred_element_type=jnp.float32,
    ).T


def exchange(tree, axis_name, distance):
    size = lax.axis_size(axis_name)
    perm = [(i, i ^ distance) for i in range(size)]
    return lax.ppermute(tree, axis_name, perm)


def butterfly(tree, axis_name):
    size = lax.axis_size(axis_name)
    distance = 1
    while distance < size:
        other = exchange(tree, axis_name, distance)
        tree = jax.tree.map(lambda a, b: a + b, tree, other)
        distance *= 2
    return tree


def local(
    in_inputs,
    in_cotangents,
    out_inputs,
    out_cotangents,
    token_counts,
    in_error,
    out_error,
    in_query,
    out_query,
    vec_grads,
    in_weight,
    in_moment,
    out_weight,
    out_moment,
    vec_weight,
    vec_moment,
):
    highest = lax.Precision.HIGHEST
    replicas = lax.axis_size("shards")
    shard_index = lax.axis_index("shards")
    position = jnp.arange(in_inputs.shape[3], dtype=jnp.int32)
    valid = (position[None, :] < token_counts[0][:, None]).astype(jnp.bfloat16)
    grad_in = gradient(in_inputs, in_cotangents, valid)
    grad_out = gradient(out_inputs, out_cotangents, valid)
    grad_q_in = jnp.dot(grad_in, in_query[0], precision=highest)
    error_q_in = jnp.dot(in_error[0, 0], in_query[0], precision=highest)
    grad_q_out = jnp.dot(grad_out, out_query[0], precision=highest)
    error_q_out = jnp.dot(out_error[0, 0], out_query[0], precision=highest)
    vec_len = vec_grads.shape[-1]
    count = jnp.sum(token_counts).astype(jnp.float32)
    summed = butterfly(jnp.concatenate([vec_grads[0, 0], count[None]]), "shards")
    vec_total = summed[:vec_len]
    total = summed[vec_len]
    core = lax.axis_index("tensor")
    half = grad_q_in.shape[0] // 2
    pair = jnp.stack([grad_q_in, error_q_in])
    keep = lax.dynamic_slice_in_dim(pair, core * half, half, 1)
    give = lax.dynamic_slice_in_dim(pair, (1 - core) * half, half, 1)
    pair = keep + exchange(give, "tensor", 1)
    part_in = pair[0] / total + pair[1]
    part_out = grad_q_out / total + error_q_out
    part_in, left_out = butterfly((part_in, part_out), "shards")
    other = exchange(jnp.concatenate([part_in, left_out], axis=0), "tensor", 1)
    other_in = other[:half]
    other_out = other[half:]
    left_in = jnp.where(
        core == 0,
        jnp.concatenate([part_in, other_in], axis=0),
        jnp.concatenate([other_in, part_in], axis=0),
    )
    gram_in = jnp.dot(left_in.T, left_in, precision=highest)
    gram_out = jnp.dot(left_out.T, left_out, precision=highest) + jnp.dot(
        other_out.T, other_out, precision=highest
    )
    ortho = triangular_apply(jnp.stack([left_in, left_out]), jnp.stack([gram_in, gram_out]))
    ortho_in = ortho[0]
    ortho_out = ortho[1]
    work_in = grad_in / total + in_error[0, 0]
    work_out = grad_out / total + out_error[0, 0]
    right_part_in = jnp.dot(ortho_in.T, work_in, precision=highest)
    right_part_out = jnp.dot(ortho_out.T, work_out, precision=highest)
    width = right_part_out.shape[1] // 2
    keep = lax.dynamic_slice_in_dim(right_part_out, core * width, width, 1)
    give = lax.dynamic_slice_in_dim(right_part_out, (1 - core) * width, width, 1)
    out_half = keep + exchange(give, "tensor", 1)
    right_in, out_half = butterfly((right_part_in, out_half), "shards")
    right_in = right_in / replicas
    out_half = out_half / replicas
    vec_mean = vec_total / total
    own_square = (
        jnp.sum(right_in * right_in) + jnp.sum(vec_mean * vec_mean) + jnp.sum(out_half * out_half)
    )
    own_square, right_in, out_half = lax.optimization_barrier((own_square, right_in, out_half))
    other_half = exchange(out_half, "tensor", 1)
    right_out = jnp.where(
        core == 0,
        jnp.concatenate([out_half, other_half], axis=1),
        jnp.concatenate([other_half, out_half], axis=1),
    )
    square_sum = butterfly(butterfly(own_square, "tensor"), "sections")
    approx_in = jnp.dot(ortho_in, right_in, precision=highest)
    approx_out = jnp.dot(ortho_out, right_out, precision=highest)
    new_in_error = (work_in - approx_in)[None, None]
    new_out_error = (work_out - approx_out)[None, None]
    factor = 1024.0 / jnp.sqrt(square_sum + 1e-06)
    row_count = in_weight.shape[1]
    shard_in = lax.dynamic_slice_in_dim(approx_in, shard_index * row_count, row_count, 0)
    col_count = out_weight.shape[2]
    shard_out = lax.dynamic_slice_in_dim(approx_out, shard_index * col_count, col_count, 1)
    new_in_moment = 0.9 * in_moment + factor * shard_in[None]
    new_out_moment = 0.9 * out_moment + factor * shard_out[None]
    new_vec_moment = 0.9 * vec_moment + factor * vec_mean[None]
    return (
        new_in_error,
        new_out_error,
        in_weight - 0.1 * new_in_moment,
        new_in_moment,
        out_weight - 0.1 * new_out_moment,
        new_out_moment,
        vec_weight - 0.1 * new_vec_moment,
        new_vec_moment,
    )


def solution(mesh):
    return jax.shard_map(
        local,
        mesh=mesh,
        in_specs=(
            P("sections", "shards", None, None, None),
            P("sections", "shards", None, None, "tensor"),
            P("sections", "shards", None, None, "tensor"),
            P("sections", "shards", None, None, None),
            P("shards", None),
            P("sections", "shards", None, "tensor"),
            P("sections", "shards", "tensor", None),
            P("sections", "tensor", None),
            P("sections", None, None),
            P("sections", "shards", "tensor"),
            P("sections", "shards", "tensor"),
            P("sections", "shards", "tensor"),
            P("sections", "tensor", "shards"),
            P("sections", "tensor", "shards"),
            P("sections", "tensor"),
            P("sections", "tensor"),
        ),
        out_specs=(
            P("sections", "shards", None, "tensor"),
            P("sections", "shards", "tensor", None),
            P("sections", "shards", "tensor"),
            P("sections", "shards", "tensor"),
            P("sections", "tensor", "shards"),
            P("sections", "tensor", "shards"),
            P("sections", "tensor"),
            P("sections", "tensor"),
        ),
        check_vma=False,
    )
```

```python
import jax
import jax.numpy as jnp
from jax import lax
from jax.sharding import PartitionSpec as P


def triangular_apply(left, gram):
    factor = jnp.linalg.cholesky(gram)
    solved = jax.scipy.linalg.solve_triangular(factor, jnp.swapaxes(left, -1, -2), lower=True)
    return jnp.swapaxes(solved, -1, -2)


def gradient(inputs, cotangents, valid):
    width_a = inputs.shape[-1]
    width_b = cotangents.shape[-1]
    masked = cotangents[0, 0] * valid[..., None]
    return lax.dot_general(
        masked.reshape(-1, width_b),
        inputs[0, 0].reshape(-1, width_a),
        (((0,), (0,)), ((), ())),
        preferred_element_type=jnp.float32,
    ).T


def exchange(tree, axis_name, distance):
    size = lax.axis_size(axis_name)
    perm = [(i, i ^ distance) for i in range(size)]
    return lax.ppermute(tree, axis_name, perm)


def butterfly(tree, axis_name):
    size = lax.axis_size(axis_name)
    distance = 1
    while distance < size:
        other = exchange(tree, axis_name, distance)
        tree = jax.tree.map(lambda a, b: a + b, tree, other)
        distance *= 2
    return tree


def ordered_total(value, axis_name):
    size = lax.axis_size(axis_name)
    index = lax.axis_index(axis_name)
    got = [value]
    for shift in range(1, size):
        perm = [(i, (i + shift) % size) for i in range(size)]
        got.append(lax.ppermute(value, axis_name, perm))
    stacked = jnp.stack(got)
    ordered = stacked[(index - jnp.arange(size)) % size]
    result = ordered[0]
    for j in range(1, size):
        result = result + ordered[j]
    return result


def local(
    in_inputs,
    in_cotangents,
    out_inputs,
    out_cotangents,
    token_counts,
    in_error,
    out_error,
    in_query,
    out_query,
    vec_grads,
    in_weight,
    in_moment,
    out_weight,
    out_moment,
    vec_weight,
    vec_moment,
):
    highest = lax.Precision.HIGHEST
    replicas = lax.axis_size("shards")
    shard_index = lax.axis_index("shards")
    position = jnp.arange(in_inputs.shape[3], dtype=jnp.int32)
    valid = (position[None, :] < token_counts[0][:, None]).astype(jnp.bfloat16)
    grad_in = gradient(in_inputs, in_cotangents, valid)
    grad_out = gradient(out_inputs, out_cotangents, valid)
    grad_q_in = jnp.dot(grad_in, in_query[0], precision=highest)
    error_q_in = jnp.dot(in_error[0, 0], in_query[0], precision=highest)
    grad_q_out = jnp.dot(grad_out, out_query[0], precision=highest)
    error_q_out = jnp.dot(out_error[0, 0], out_query[0], precision=highest)
    vec_len = vec_grads.shape[-1]
    count = jnp.sum(token_counts).astype(jnp.float32)
    summed = butterfly(jnp.concatenate([vec_grads[0, 0], count[None]]), "shards")
    vec_total = summed[:vec_len]
    total = summed[vec_len]
    part_in = grad_q_in / total + error_q_in
    part_out = grad_q_out / total + error_q_out
    part_in, left_out = butterfly((part_in, part_out), "shards")
    rank = part_in.shape[1]
    other = exchange(jnp.concatenate([part_in, left_out], axis=1), "tensor", 1)
    left_in = part_in + other[:, :rank]
    other_out = other[:, rank:]
    gram_in = jnp.dot(left_in.T, left_in, precision=highest)
    gram_out = jnp.dot(left_out.T, left_out, precision=highest) + jnp.dot(
        other_out.T, other_out, precision=highest
    )
    ortho = triangular_apply(jnp.stack([left_in, left_out]), jnp.stack([gram_in, gram_out]))
    ortho_in = ortho[0]
    ortho_out = ortho[1]
    work_in = grad_in / total + in_error[0, 0]
    work_out = grad_out / total + out_error[0, 0]
    right_part_in = jnp.dot(ortho_in.T, work_in, precision=highest)
    right_part_out = jnp.dot(ortho_out.T, work_out, precision=highest)
    right_part_out = right_part_out + exchange(right_part_out, "tensor", 1)
    right_in, right_out = butterfly((right_part_in, right_part_out), "shards")
    right_in = right_in / replicas
    right_out = right_out / replicas
    vec_mean = vec_total / total
    own_square = jnp.sum(right_in * right_in) + jnp.sum(vec_mean * vec_mean)
    out_square = jnp.sum(right_out * right_out)
    own_square = own_square + jnp.where(lax.axis_index("tensor") == 0, out_square, 0.0)
    own_square, right_in, right_out = lax.optimization_barrier((own_square, right_in, right_out))
    square_sum = butterfly(ordered_total(own_square, "sections"), "tensor")
    approx_in = jnp.dot(ortho_in, right_in, precision=highest)
    approx_out = jnp.dot(ortho_out, right_out, precision=highest)
    new_in_error = (work_in - approx_in)[None, None]
    new_out_error = (work_out - approx_out)[None, None]
    factor = 1024.0 / jnp.sqrt(square_sum + 1e-06)
    row_count = in_weight.shape[1]
    shard_in = lax.dynamic_slice_in_dim(approx_in, shard_index * row_count, row_count, 0)
    col_count = out_weight.shape[2]
    shard_out = lax.dynamic_slice_in_dim(approx_out, shard_index * col_count, col_count, 1)
    new_in_moment = 0.9 * in_moment + factor * shard_in[None]
    new_out_moment = 0.9 * out_moment + factor * shard_out[None]
    new_vec_moment = 0.9 * vec_moment + factor * vec_mean[None]
    return (
        new_in_error,
        new_out_error,
        in_weight - 0.1 * new_in_moment,
        new_in_moment,
        out_weight - 0.1 * new_out_moment,
        new_out_moment,
        vec_weight - 0.1 * new_vec_moment,
        new_vec_moment,
    )


def solution(mesh):
    return jax.shard_map(
        local,
        mesh=mesh,
        in_specs=(
            P("sections", "shards", None, None, None),
            P("sections", "shards", None, None, "tensor"),
            P("sections", "shards", None, None, "tensor"),
            P("sections", "shards", None, None, None),
            P("shards", None),
            P("sections", "shards", None, "tensor"),
            P("sections", "shards", "tensor", None),
            P("sections", "tensor", None),
            P("sections", None, None),
            P("sections", "shards", "tensor"),
            P("sections", "shards", "tensor"),
            P("sections", "shards", "tensor"),
            P("sections", "tensor", "shards"),
            P("sections", "tensor", "shards"),
            P("sections", "tensor"),
            P("sections", "tensor"),
        ),
        out_specs=(
            P("sections", "shards", None, "tensor"),
            P("sections", "shards", "tensor", None),
            P("sections", "shards", "tensor"),
            P("sections", "shards", "tensor"),
            P("sections", "tensor", "shards"),
            P("sections", "tensor", "shards"),
            P("sections", "tensor"),
            P("sections", "tensor"),
        ),
        check_vma=False,
    )
```

```python
import jax
import jax.numpy as jnp
from jax import lax
from jax.sharding import PartitionSpec as P


def triangular_apply(left, gram):
    factor = jnp.linalg.cholesky(gram)
    solved = jax.scipy.linalg.solve_triangular(factor, jnp.swapaxes(left, -1, -2), lower=True)
    return jnp.swapaxes(solved, -1, -2)


def gradient(inputs, cotangents, valid):
    width_a = inputs.shape[-1]
    width_b = cotangents.shape[-1]
    masked = cotangents[0, 0] * valid[..., None]
    return lax.dot_general(
        inputs[0, 0].reshape(-1, width_a),
        masked.reshape(-1, width_b),
        (((0,), (0,)), ((), ())),
        preferred_element_type=jnp.float32,
    )


def partner(position, distance, low_bits=3):
    def gray(value):
        return value ^ (value >> 1)

    def inverse_gray(value):
        result = 0
        while value:
            result ^= value
            value >>= 1
        return result

    low = (1 << low_bits) - 1
    label = (inverse_gray(position >> low_bits) << low_bits) | (position & low)
    label ^= distance
    return (gray(label >> low_bits) << low_bits) | (label & low)


def exchange(tree, axis_name, distance):
    size = lax.axis_size(axis_name)
    perm = [(i, partner(i, distance)) for i in range(size)]
    return lax.ppermute(tree, axis_name, perm)


def butterfly(tree, axis_name):
    size = lax.axis_size(axis_name)
    distance = 1
    while distance < size:
        other = exchange(tree, axis_name, distance)
        tree = jax.tree.map(lambda a, b: a + b, tree, other)
        distance *= 2
    return tree


def local(
    in_inputs,
    in_cotangents,
    out_inputs,
    out_cotangents,
    token_counts,
    in_error,
    out_error,
    in_query,
    out_query,
    vec_grads,
    in_weight,
    in_moment,
    out_weight,
    out_moment,
    vec_weight,
    vec_moment,
):
    highest = lax.Precision.HIGHEST
    contract = (((0,), (0,)), ((), ()))
    replicas = lax.axis_size("shards")
    shard_index = lax.axis_index("shards")
    position = jnp.arange(in_inputs.shape[3], dtype=jnp.int32)
    valid = (position[None, :] < token_counts[0][:, None]).astype(jnp.bfloat16)
    grad_in = gradient(in_inputs, in_cotangents, valid)
    grad_out = gradient(out_inputs, out_cotangents, valid)
    grad_q_in = jnp.dot(grad_in, in_query[0], precision=highest)
    error_q_in = jnp.dot(in_error[0, 0], in_query[0], precision=highest)
    grad_q_out = jnp.dot(grad_out, out_query[0], precision=highest)
    error_q_out = jnp.dot(out_error[0, 0], out_query[0], precision=highest)
    vec_len = vec_grads.shape[-1]
    count = jnp.sum(token_counts).astype(jnp.float32)
    summed = butterfly(jnp.concatenate([vec_grads[0, 0], count[None]]), "shards")
    vec_total = summed[:vec_len]
    total = summed[vec_len]
    part_in = grad_q_in / total + error_q_in
    part_out = grad_q_out / total + error_q_out
    part_in, left_out = butterfly((part_in, part_out), "shards")
    rank = part_in.shape[1]
    other = exchange(jnp.concatenate([part_in, left_out], axis=1), "tensor", 1)
    left_in = part_in + other[:, :rank]
    other_out = other[:, rank:]
    gram_in = jnp.dot(left_in.T, left_in, precision=highest)
    gram_out = jnp.dot(left_out.T, left_out, precision=highest) + jnp.dot(
        other_out.T, other_out, precision=highest
    )
    ortho = triangular_apply(jnp.stack([left_in, left_out]), jnp.stack([gram_in, gram_out]))
    ortho_in = ortho[0]
    ortho_out = ortho[1]
    work_in = grad_in / total + in_error[0, 0]
    work_out = grad_out / total + out_error[0, 0]
    right_part_in = lax.dot_general(work_in, ortho_in, contract, precision=highest)
    right_part_out = lax.dot_general(work_out, ortho_out, contract, precision=highest)
    right_part_out = right_part_out + exchange(right_part_out, "tensor", 1)
    right_in, right_out = butterfly((right_part_in, right_part_out), "shards")
    right_in = right_in / replicas
    right_out = right_out / replicas
    vec_mean = vec_total / total
    own_square = jnp.sum(right_in * right_in) + jnp.sum(vec_mean * vec_mean)
    out_square = jnp.sum(right_out * right_out)
    own_square = own_square + jnp.where(lax.axis_index("tensor") == 0, out_square, 0.0)
    square_sum = butterfly(butterfly(own_square, "tensor"), "sections")
    approx_in = jnp.dot(ortho_in, right_in.T, precision=highest)
    approx_out = jnp.dot(ortho_out, right_out.T, precision=highest)
    new_in_error = (work_in - approx_in)[None, None]
    new_out_error = (work_out - approx_out)[None, None]
    factor = 1024.0 / jnp.sqrt(square_sum + 1e-06)
    row_count = in_weight.shape[1]
    shard_in = lax.dynamic_slice_in_dim(approx_in, shard_index * row_count, row_count, 0)
    col_count = out_weight.shape[2]
    shard_out = lax.dynamic_slice_in_dim(approx_out, shard_index * col_count, col_count, 1)
    new_in_moment = 0.9 * in_moment + factor * shard_in[None]
    new_out_moment = 0.9 * out_moment + factor * shard_out[None]
    new_vec_moment = 0.9 * vec_moment + factor * vec_mean[None]
    return (
        new_in_error,
        new_out_error,
        in_weight - 0.1 * new_in_moment,
        new_in_moment,
        out_weight - 0.1 * new_out_moment,
        new_out_moment,
        vec_weight - 0.1 * new_vec_moment,
        new_vec_moment,
    )


def solution(mesh):
    return jax.shard_map(
        local,
        mesh=mesh,
        in_specs=(
            P("sections", "shards", None, None, None),
            P("sections", "shards", None, None, "tensor"),
            P("sections", "shards", None, None, "tensor"),
            P("sections", "shards", None, None, None),
            P("shards", None),
            P("sections", "shards", None, "tensor"),
            P("sections", "shards", "tensor", None),
            P("sections", "tensor", None),
            P("sections", None, None),
            P("sections", "shards", "tensor"),
            P("sections", "shards", "tensor"),
            P("sections", "shards", "tensor"),
            P("sections", "tensor", "shards"),
            P("sections", "tensor", "shards"),
            P("sections", "tensor"),
            P("sections", "tensor"),
        ),
        out_specs=(
            P("sections", "shards", None, "tensor"),
            P("sections", "shards", "tensor", None),
            P("sections", "shards", "tensor"),
            P("sections", "shards", "tensor"),
            P("sections", "tensor", "shards"),
            P("sections", "tensor", "shards"),
            P("sections", "tensor"),
            P("sections", "tensor"),
        ),
        check_vma=False,
    )
```

```python
import jax
import jax.numpy as jnp
from jax import lax
from jax.sharding import PartitionSpec as P


def triangular_apply(left, gram):
    factor = jnp.linalg.cholesky(gram)
    solved = jax.scipy.linalg.solve_triangular(factor, jnp.swapaxes(left, -1, -2), lower=True)
    return jnp.swapaxes(solved, -1, -2)


def gradient(inputs, cotangents, valid):
    width_a = inputs.shape[-1]
    width_b = cotangents.shape[-1]
    masked = cotangents[0, 0] * valid[..., None]
    return lax.dot_general(
        inputs[0, 0].reshape(-1, width_a),
        masked.reshape(-1, width_b),
        (((0,), (0,)), ((), ())),
        preferred_element_type=jnp.float32,
    )


def partner(position, distance, low_bits=3):
    def gray(value):
        return value ^ (value >> 1)

    def inverse_gray(value):
        result = 0
        while value:
            result ^= value
            value >>= 1
        return result

    low = (1 << low_bits) - 1
    label = (inverse_gray(position >> low_bits) << low_bits) | (position & low)
    label ^= distance
    return (gray(label >> low_bits) << low_bits) | (label & low)


def neighbour(position, low_bits=3):
    ring = 1 << low_bits
    low = position % ring
    other = (low + 1) % ring if low % 2 else (low - 1) % ring
    return position - low + other


def exchange(tree, axis_name, distance, shifted=False):
    size = lax.axis_size(axis_name)
    if shifted:
        perm = [(i, neighbour(i)) for i in range(size)]
    else:
        perm = [(i, partner(i, distance)) for i in range(size)]
    return lax.ppermute(tree, axis_name, perm)


def butterfly(tree, axis_name, shifted=False):
    size = lax.axis_size(axis_name)
    distance = 1
    while distance < size:
        other = exchange(tree, axis_name, distance, shifted and distance == 2)
        tree = jax.tree.map(lambda a, b: a + b, tree, other)
        distance *= 2
    return tree


def local(
    in_inputs,
    in_cotangents,
    out_inputs,
    out_cotangents,
    token_counts,
    in_error,
    out_error,
    in_query,
    out_query,
    vec_grads,
    in_weight,
    in_moment,
    out_weight,
    out_moment,
    vec_weight,
    vec_moment,
):
    highest = lax.Precision.HIGHEST
    contract = (((0,), (0,)), ((), ()))
    replicas = lax.axis_size("shards")
    shard_index = lax.axis_index("shards")
    position = jnp.arange(in_inputs.shape[3], dtype=jnp.int32)
    valid = (position[None, :] < token_counts[0][:, None]).astype(jnp.bfloat16)
    grad_in = gradient(in_inputs, in_cotangents, valid)
    grad_out = gradient(out_inputs, out_cotangents, valid)
    grad_q_in = jnp.dot(grad_in, in_query[0], precision=highest)
    error_q_in = jnp.dot(in_error[0, 0], in_query[0], precision=highest)
    grad_q_out = jnp.dot(grad_out, out_query[0], precision=highest)
    error_q_out = jnp.dot(out_error[0, 0], out_query[0], precision=highest)
    vec_len = vec_grads.shape[-1]
    count = jnp.sum(token_counts).astype(jnp.float32)
    summed = butterfly(jnp.concatenate([vec_grads[0, 0], count[None]]), "shards")
    vec_total = summed[:vec_len]
    total = summed[vec_len]
    part_in = grad_q_in / total + error_q_in
    part_out = grad_q_out / total + error_q_out
    part_in, left_out = butterfly((part_in, part_out), "shards", shifted=True)
    rank = part_in.shape[1]
    other = exchange(jnp.concatenate([part_in, left_out], axis=1), "tensor", 1)
    left_in = part_in + other[:, :rank]
    other_out = other[:, rank:]
    gram_in = jnp.dot(left_in.T, left_in, precision=highest)
    gram_out = jnp.dot(left_out.T, left_out, precision=highest) + jnp.dot(
        other_out.T, other_out, precision=highest
    )
    ortho = triangular_apply(jnp.stack([left_in, left_out]), jnp.stack([gram_in, gram_out]))
    ortho_in = ortho[0]
    ortho_out = ortho[1]
    work_in = grad_in / total + in_error[0, 0]
    work_out = grad_out / total + out_error[0, 0]
    right_part_in = lax.dot_general(work_in, ortho_in, contract, precision=highest)
    right_part_out = lax.dot_general(work_out, ortho_out, contract, precision=highest)
    right_part_out = right_part_out + exchange(right_part_out, "tensor", 1)
    right_in, right_out = butterfly((right_part_in, right_part_out), "shards")
    right_in = right_in / replicas
    right_out = right_out / replicas
    vec_mean = vec_total / total
    own_square = jnp.sum(right_in * right_in) + jnp.sum(vec_mean * vec_mean)
    out_square = jnp.sum(right_out * right_out)
    own_square = own_square + jnp.where(lax.axis_index("tensor") == 0, out_square, 0.0)
    square_sum = butterfly(butterfly(own_square, "tensor"), "sections")
    approx_in = jnp.dot(ortho_in, right_in.T, precision=highest)
    approx_out = jnp.dot(ortho_out, right_out.T, precision=highest)
    new_in_error = (work_in - approx_in)[None, None]
    new_out_error = (work_out - approx_out)[None, None]
    factor = 1024.0 / jnp.sqrt(square_sum + 1e-06)
    row_count = in_weight.shape[1]
    shard_in = lax.dynamic_slice_in_dim(approx_in, shard_index * row_count, row_count, 0)
    col_count = out_weight.shape[2]
    shard_out = lax.dynamic_slice_in_dim(approx_out, shard_index * col_count, col_count, 1)
    new_in_moment = 0.9 * in_moment + factor * shard_in[None]
    new_out_moment = 0.9 * out_moment + factor * shard_out[None]
    new_vec_moment = 0.9 * vec_moment + factor * vec_mean[None]
    return (
        new_in_error,
        new_out_error,
        in_weight - 0.1 * new_in_moment,
        new_in_moment,
        out_weight - 0.1 * new_out_moment,
        new_out_moment,
        vec_weight - 0.1 * new_vec_moment,
        new_vec_moment,
    )


def solution(mesh):
    return jax.shard_map(
        local,
        mesh=mesh,
        in_specs=(
            P("sections", "shards", None, None, None),
            P("sections", "shards", None, None, "tensor"),
            P("sections", "shards", None, None, "tensor"),
            P("sections", "shards", None, None, None),
            P("shards", None),
            P("sections", "shards", None, "tensor"),
            P("sections", "shards", "tensor", None),
            P("sections", "tensor", None),
            P("sections", None, None),
            P("sections", "shards", "tensor"),
            P("sections", "shards", "tensor"),
            P("sections", "shards", "tensor"),
            P("sections", "tensor", "shards"),
            P("sections", "tensor", "shards"),
            P("sections", "tensor"),
            P("sections", "tensor"),
        ),
        out_specs=(
            P("sections", "shards", None, "tensor"),
            P("sections", "shards", "tensor", None),
            P("sections", "shards", "tensor"),
            P("sections", "shards", "tensor"),
            P("sections", "tensor", "shards"),
            P("sections", "tensor", "shards"),
            P("sections", "tensor"),
            P("sections", "tensor"),
        ),
        check_vma=False,
    )
```
